32 devices in a mesh: grp: 2 (over x), spec: 16 (over z, y, core).
Axes of the slice: x: 2, y: 2, z: 4, core: 2. Of those that a mesh axis runs over, the one named last changes fastest.
Arguments:
- lower_coef: bfloat16 [64, 196, 1024], P(('grp', 'spec')), parts along dimension 0, may hold values from -6 to 6
- upper_coef: bfloat16 [64, 196, 1024], P(('grp', 'spec')), parts along dimension 0, may hold values from -6 to 6
- w_down: bfloat16 [4096, 1024], P('spec'), may hold values from -0.09375 to 0.09375
- w_up: bfloat16 [4096, 1024], P('spec'), may hold values from -0.1875 to 0.1875
- pw1_bias: bfloat16 [4096], P('spec'), may hold values from -0.059814453 to 0.059814453
- slopes: bfloat16 [8192, 2, 196], P(('grp', 'spec')), parts along dimension 0, may hold values from -0.099609375 to 1.09375
- intercepts: bfloat16 [8192, 2, 196], P(('grp', 'spec')), parts along dimension 0, may hold values from -0.019897461 to 0.019897461
- ln_scale: float32 [392], P('grp'), parts along dimension 0, may hold values from 0.3 to 3
- box_center: float32 [392, 1024], P('grp', 'spec'), parts along dimension 0, may hold values from -0.03 to 0.03
- box_radius: float32 [392, 1024], P('grp', 'spec'), parts along dimension 0, may hold values from 1e-06 to 0.0001
- dw_weight: float32 [49, 1024], P(None, 'spec'), may hold values from -0.875 to 0.875
- dw_bias: float32 [1024], P('spec'), may hold values from -0.06 to 0.06
- ln_gain: float32 [1024], P('spec'), may hold values from 0.5 to 1.5
- ln_bias: float32 [1024], P('spec'), may hold values from -0.06 to 0.06
- ls_gamma: float32 [1024], P('spec'), may hold values from 0.1 to 1
- pw2_bias: float32 [1024], P('spec'), may hold values from -0.06 to 0.06
Outputs:
- lower_input: bfloat16 [64, 196, 1024], P(('grp', 'spec')), parts along dimension 0
- upper_input: bfloat16 [64, 196, 1024], P(('grp', 'spec')), parts along dimension 0
- bounds: float32 [64, 2], P(('grp', 'spec')), parts along dimension 0
The draws below stay inside these ranges and needn't reach their ends.
There are 2 independent parts, one for each index of `grp`. The reference program is written for one: setup_inputs(seed, part) draws one part's arguments, and reference() takes and returns one part's arrays. A program takes and returns all parts, laid end to end along the dimension named above; an argument that names none is the same for every part. Nothing has to cross between parts.
All inputs are finite; a program needn't handle non-finite values.
Results may differ from the reference program's by a relative error of at most 0.0039.
Values may be sent and summed in bfloat16 or wider, within the bound.
No kernel may reach another device: no remote copies, remote signals or barrier semaphores. Data moves between devices by JAX's collectives and lax.ppermute only.
A program may use at most 192 MiB of HBM per device.

```python
import math
import jax
import jax.numpy as jnp
from jax import lax

C = 1024
HID = 4096
MAP = 14
KERNEL = 7
PIX = 196
SPECS = 32


def block_levels(own_key, dims, shards, smallest, top_value):
    level = 1.0
    for axis_at, parts in shards:
        draws = jax.random.uniform(jax.random.fold_in(jax.random.fold_in(own_key, 6), axis_at), (parts,), jnp.float32, smallest / len(shards), top_value / len(shards))
        level = level * jnp.repeat(jnp.exp(draws), dims[axis_at] // parts).reshape((-1,) + (1,) * (len(dims) - 1 - axis_at))
    return level


def normal_values(key, shape, deviation, limit, shards=(), kind=jnp.bfloat16):
    entries = jax.random.normal(key, shape, jnp.float32) * deviation
    if len(shards) > 0:
        entries = block_levels(key, shape, shards, -0.22, 0.18) * entries
    return jnp.clip(entries, min=-limit, max=limit).astype(kind)


def setup_inputs(seed: int = 0, part: int = 0) -> dict:
    key_list = jax.random.split(jax.random.key(seed), 17)
    own_keys = jax.random.split(jax.random.fold_in(key_list[16], part), 17)
    lower_coef = normal_values(own_keys[0], (SPECS, PIX, C), 1.0, 6.0, ((0, 16),))
    upper_coef = normal_values(own_keys[1], (SPECS, PIX, C), 1.0, 6.0, ((0, 16),))
    w_down = normal_values(key_list[2], (HID, C), HID ** -0.5, 0.09375, ((0, 16),))
    w_up = normal_values(key_list[3], (HID, C), C ** -0.5, 0.1875, ((0, 16),))
    pw1_bias = normal_values(key_list[4], (HID,), 0.01, 0.059814453, ((0, 16),))
    slopes = jnp.clip(-0.099609375 + 1.1933594 * jax.random.uniform(own_keys[5], (HID, 2, PIX), jnp.float32) ** block_levels(own_keys[5], (HID, 2, PIX), ((0, 16),), -0.2, 0.2), -0.099609375, 1.09375).astype(jnp.bfloat16)
    intercepts = jnp.clip(jax.random.uniform(own_keys[6], (HID, 2, PIX), jnp.float32, -0.019897461, 0.019897461) * block_levels(own_keys[6], (HID, 2, PIX), ((0, 16),), -0.4, 0.0), -0.019897461, 0.019897461).astype(jnp.bfloat16)
    ln_scale = jnp.clip(jnp.exp(jax.random.uniform(own_keys[7], (PIX,), jnp.float32, math.log(0.3), math.log(3.0))), 0.3, 3.0)
    box_center = normal_values(own_keys[8], (PIX, C), 0.005, 0.03, ((1, 16),), jnp.float32)
    box_radius = jnp.clip(jnp.exp(math.log(0.0001) - 4.6051702 * jax.random.uniform(own_keys[9], (PIX, C), jnp.float32) ** block_levels(own_keys[9], (PIX, C), ((1, 16),), -0.2, 0.2)), 9.999999974752427e-07, 0.0001)
    dw_weight = normal_values(key_list[10], (KERNEL * KERNEL, C), (KERNEL * KERNEL) ** -0.5, 0.875, ((1, 16),), jnp.float32)
    dw_bias = normal_values(key_list[11], (C,), 0.01, 0.06, ((0, 16),), jnp.float32)
    ln_gain = jnp.clip(1.0 + 0.1 * jax.random.normal(key_list[12], (C,), jnp.float32), 0.5, 1.5)
    ln_bias = normal_values(key_list[13], (C,), 0.01, 0.06, ((0, 16),), jnp.float32)
    ls_gamma = jnp.clip(jnp.exp(math.log(1.0) - 2.3025851 * jax.random.uniform(key_list[14], (C,), jnp.float32) ** block_levels(key_list[14], (C,), ((0, 16),), -0.2, 0.2)), 0.1, 1.0)
    pw2_bias = normal_values(key_list[15], (C,), 0.01, 0.06, ((0, 16),), jnp.float32)
    return {"lower_coef": lower_coef, "upper_coef": upper_coef, "w_down": w_down, "w_up": w_up, "pw1_bias": pw1_bias, "slopes": slopes, "intercepts": intercepts, "ln_scale": ln_scale, "box_center": box_center, "box_radius": box_radius, "dw_weight": dw_weight, "dw_bias": dw_bias, "ln_gain": ln_gain, "ln_bias": ln_bias, "ls_gamma": ls_gamma, "pw2_bias": pw2_bias}


def conv_back(centered, taps):
    half = KERNEL // 2
    padded = jnp.pad(centered, ((0, 0), (half, half), (half, half), (0, 0)))
    result = jnp.zeros(centered.shape, jnp.float32)
    for row_off in range(KERNEL):
        for col_off in range(KERNEL):
            window = padded[:, 2 * half - row_off:2 * half - row_off + MAP, 2 * half - col_off:2 * half - col_off + MAP, :]
            result = result + window * taps[row_off, col_off]
    return result


def reference(lower_coef, upper_coef, w_down, w_up, pw1_bias, slopes, intercepts, ln_scale, box_center, box_radius, dw_weight, dw_bias, ln_gain, ln_bias, ls_gamma, pw2_bias):
    slope_maps = slopes.astype(jnp.float32).transpose(1, 2, 0)
    icpt_maps = intercepts.astype(jnp.float32).transpose(1, 2, 0)
    first = jnp.stack([slope_maps[0], slope_maps[1]])
    second = jnp.stack([slope_maps[1], slope_maps[0]])
    first_icpt = jnp.stack([icpt_maps[0], icpt_maps[1]])
    second_icpt = jnp.stack([icpt_maps[1], icpt_maps[0]])
    hid_bias = pw1_bias.astype(jnp.float32)
    taps = dw_weight.reshape(KERNEL, KERNEL, C)

    def one_row(pair):
        coef = pair.astype(jnp.float32)
        scaled = coef * ls_gamma
        bias = jnp.sum(scaled * pw2_bias, axis=(1, 2))
        scaled16 = scaled.astype(jnp.bfloat16)
        hidden = jnp.dot(scaled16.reshape(2 * PIX, C), w_down.T, preferred_element_type=jnp.float32).reshape(2, PIX, HID)
        positive = jnp.maximum(hidden, 0.0)
        negative = jnp.minimum(hidden, 0.0)
        relaxed = positive * first + negative * second
        bias = bias + jnp.sum(positive * first_icpt + negative * second_icpt + relaxed * hid_bias, axis=(1, 2))
        relaxed16 = relaxed.astype(jnp.bfloat16)
        normed = jnp.dot(relaxed16.reshape(2 * PIX, HID), w_up, preferred_element_type=jnp.float32).reshape(2, PIX, C)
        bias = bias + jnp.sum(normed * ln_bias, axis=(1, 2))
        tilted = normed * ln_gain
        centered = ln_scale[None, :, None] * (tilted - jnp.mean(tilted, axis=-1, keepdims=True))
        bias = bias + jnp.sum(centered * dw_bias, axis=(1, 2))
        conv = conv_back(centered.reshape(2, MAP, MAP, C), taps).reshape(2, PIX, C)
        total = coef + conv
        linear = jnp.sum(total * box_center, axis=(1, 2))
        spread = jnp.sum(jnp.abs(total) * box_radius, axis=(1, 2))
        bounds = bias + linear + jnp.stack([-spread[0], spread[1]])
        return total.astype(jnp.bfloat16), bounds

    pairs = jnp.stack([lower_coef, upper_coef], axis=1)
    coefs, bounds = lax.map(one_row, pairs)
    return (coefs[:, 0], coefs[:, 1], bounds)
```

```python
import functools

import jax
import jax.numpy as jnp
from jax import lax
from jax.sharding import PartitionSpec as P

MAP = 14
KERNEL = 7


def conv_back(centered, taps):
    half = KERNEL // 2
    padded = jnp.pad(centered, ((0, 0), (half, half), (half, half), (0, 0)))
    result = jnp.zeros(centered.shape, jnp.float32)
    for row_off in range(KERNEL):
        for col_off in range(KERNEL):
            window = padded[
                :,
                2 * half - row_off : 2 * half - row_off + MAP,
                2 * half - col_off : 2 * half - col_off + MAP,
                :,
            ]
            result = result + window * taps[row_off, col_off]
    return result


def local(
    nsh,
    lower_coef,
    upper_coef,
    w_down,
    w_up,
    pw1_bias,
    slopes,
    intercepts,
    ln_scale,
    box_center,
    box_radius,
    dw_weight,
    dw_bias,
    ln_gain,
    ln_bias,
    ls_gamma,
    pw2_bias,
):
    nrows, npix, chans = lower_coef.shape
    hl = w_down.shape[0]
    cl = dw_bias.shape[0]
    ntap = dw_weight.shape[0]

    small = jnp.concatenate(
        [
            box_center,
            box_radius,
            dw_weight,
            dw_bias[None],
            ln_gain[None],
            ln_bias[None],
            ls_gamma[None],
            pw2_bias[None],
        ],
        axis=0,
    )
    nsmall = small.shape[0]
    small_g = lax.all_gather(small, "spec", axis=0, tiled=False)
    small_full = small_g.transpose(1, 0, 2).reshape(nsmall, nsh * cl)
    o = 0
    center = small_full[o : o + npix]
    o += npix
    radius = small_full[o : o + npix]
    o += npix
    kernel_taps = small_full[o : o + ntap]
    o += ntap
    conv_bias, gain, norm_bias, gamma, out_bias = (small_full[o + i] for i in range(5))

    relax = jnp.concatenate(
        [
            slopes.transpose(1, 2, 0).reshape(2 * npix, hl),
            intercepts.transpose(1, 2, 0).reshape(2 * npix, hl),
            pw1_bias[None],
        ],
        axis=0,
    )
    relax_g = lax.all_gather(relax, "spec", axis=0, tiled=False).astype(jnp.float32)

    def relax_map(i):
        return relax_g[:, i * npix : (i + 1) * npix].transpose(1, 0, 2)

    s0, s1, c0, c1 = (relax_map(i) for i in range(4))
    hid_bias = relax_g[:, 4 * npix]

    height = 2 * nrows * npix
    coef = jnp.stack([lower_coef, upper_coef]).astype(jnp.float32)
    scaled = coef * gamma
    bias = jnp.sum(scaled * out_bias, axis=(2, 3))
    flat = scaled.astype(jnp.bfloat16).reshape(height, chans)
    hidden = jnp.dot(
        flat,
        lax.all_gather(w_down, "spec", axis=0, tiled=True).T,
        preferred_element_type=jnp.float32,
    ).reshape(2, nrows, npix, nsh, hl)
    first = jnp.stack([s0, s1])[:, None]
    second = jnp.stack([s1, s0])[:, None]
    first_icpt = jnp.stack([c0, c1])[:, None]
    second_icpt = jnp.stack([c1, c0])[:, None]
    positive = jnp.maximum(hidden, 0.0)
    negative = jnp.minimum(hidden, 0.0)
    relaxed = positive * first + negative * second
    extra = jnp.sum(
        positive * first_icpt + negative * second_icpt + relaxed * hid_bias,
        axis=(2, 3, 4),
    )
    relaxed16 = relaxed.astype(jnp.bfloat16).reshape(height, -1)
    normed = jnp.dot(
        relaxed16,
        lax.all_gather(w_up, "spec", axis=0, tiled=True),
        preferred_element_type=jnp.float32,
    )
    bias = bias + extra
    normed = normed.reshape(2, nrows, npix, chans)
    bias = bias + jnp.sum(normed * norm_bias, axis=(2, 3))
    tilted = normed * gain
    centered = ln_scale[None, None, :, None] * (tilted - jnp.mean(tilted, axis=-1, keepdims=True))
    bias = bias + jnp.sum(centered * conv_bias, axis=(2, 3))
    taps = kernel_taps.reshape(KERNEL, KERNEL, chans)
    conv = conv_back(centered.reshape(2 * nrows, MAP, MAP, chans), taps).reshape(
        2, nrows, npix, chans
    )
    total = coef + conv
    linear = jnp.sum(total * center, axis=(2, 3))
    spread = jnp.sum(jnp.abs(total) * radius, axis=(2, 3))
    bounds = bias + linear + jnp.stack([-spread[0], spread[1]])
    return (total[0].astype(jnp.bfloat16), total[1].astype(jnp.bfloat16), bounds.T)


def solution(mesh):
    placed = (
        P(("grp", "spec"), None, None),
        P(("grp", "spec"), None, None),
        P("spec", None),
        P("spec", None),
        P("spec"),
        P(("grp", "spec"), None, None),
        P(("grp", "spec"), None, None),
        P("grp"),
        P("grp", "spec"),
        P("grp", "spec"),
        P(None, "spec"),
        P("spec"),
        P("spec"),
        P("spec"),
        P("spec"),
        P("spec"),
    )
    return jax.shard_map(
        functools.partial(local, mesh.shape["spec"]),
        mesh=mesh,
        in_specs=placed,
        out_specs=(
            P(("grp", "spec"), None, None),
            P(("grp", "spec"), None, None),
            P(("grp", "spec"), None),
        ),
        check_vma=False,
    )
```

```python
import functools

import jax
import jax.numpy as jnp
from jax import lax
from jax.sharding import PartitionSpec as P

MAP = 14
KERNEL = 7


def conv_back(centered, taps):
    half = KERNEL // 2
    padded = jnp.pad(centered, ((0, 0), (half, half), (half, half), (0, 0)))
    result = jnp.zeros(centered.shape, jnp.float32)
    for row_off in range(KERNEL):
        for col_off in range(KERNEL):
            window = padded[
                :,
                2 * half - row_off : 2 * half - row_off + MAP,
                2 * half - col_off : 2 * half - col_off + MAP,
                :,
            ]
            result = result + window * taps[row_off, col_off]
    return result


def local(
    nsh,
    lower_coef,
    upper_coef,
    w_down,
    w_up,
    pw1_bias,
    slopes,
    intercepts,
    ln_scale,
    box_center,
    box_radius,
    dw_weight,
    dw_bias,
    ln_gain,
    ln_bias,
    ls_gamma,
    pw2_bias,
):
    nrows, npix, chans = lower_coef.shape
    hl = w_down.shape[0]
    cl = dw_bias.shape[0]
    ntap = dw_weight.shape[0]

    small = jnp.concatenate(
        [
            dw_weight,
            dw_bias[None],
            ln_gain[None],
            ln_bias[None],
            ls_gamma[None],
            pw2_bias[None],
        ],
        axis=0,
    )
    nsmall = small.shape[0]
    small_g = lax.all_gather(small, "spec", axis=0, tiled=False)
    small_full = small_g.transpose(1, 0, 2).reshape(nsmall, nsh * cl)
    kernel_taps = small_full[:ntap]
    conv_bias, gain, norm_bias, gamma, out_bias = (small_full[ntap + i] for i in range(5))

    relax = jnp.concatenate(
        [
            slopes.transpose(1, 2, 0).reshape(2 * npix, hl),
            intercepts.transpose(1, 2, 0).reshape(2 * npix, hl),
            pw1_bias[None],
        ],
        axis=0,
    )
    relax_g = lax.all_gather(relax, "spec", axis=0, tiled=False).astype(jnp.float32)

    def relax_map(i):
        return relax_g[:, i * npix : (i + 1) * npix].transpose(1, 0, 2)

    s0, s1, c0, c1 = (relax_map(i) for i in range(4))
    hid_bias = relax_g[:, 4 * npix]

    height = 2 * nrows * npix
    coef = jnp.stack([lower_coef, upper_coef]).astype(jnp.float32)
    scaled = coef * gamma
    bias = jnp.sum(scaled * out_bias, axis=(2, 3))
    flat = scaled.astype(jnp.bfloat16).reshape(height, chans)
    hidden = jnp.dot(
        flat,
        lax.all_gather(w_down, "spec", axis=0, tiled=True).T,
        preferred_element_type=jnp.float32,
    ).reshape(2, nrows, npix, nsh, hl)
    first = jnp.stack([s0, s1])[:, None]
    second = jnp.stack([s1, s0])[:, None]
    first_icpt = jnp.stack([c0, c1])[:, None]
    second_icpt = jnp.stack([c1, c0])[:, None]
    positive = jnp.maximum(hidden, 0.0)
    negative = jnp.minimum(hidden, 0.0)
    relaxed = positive * first + negative * second
    extra = jnp.sum(
        positive * first_icpt + negative * second_icpt + relaxed * hid_bias,
        axis=(2, 3, 4),
    )
    relaxed16 = relaxed.astype(jnp.bfloat16).reshape(height, -1)
    normed = jnp.dot(
        relaxed16,
        lax.all_gather(w_up, "spec", axis=0, tiled=True),
        preferred_element_type=jnp.float32,
    )
    bias = bias + extra
    normed = normed.reshape(2, nrows, npix, chans)
    bias = bias + jnp.sum(normed * norm_bias, axis=(2, 3))
    tilted = normed * gain
    centered = ln_scale[None, None, :, None] * (tilted - jnp.mean(tilted, axis=-1, keepdims=True))
    bias = bias + jnp.sum(centered * conv_bias, axis=(2, 3))
    taps = kernel_taps.reshape(KERNEL, KERNEL, 1, chans)[::-1, ::-1]
    half = KERNEL // 2
    conv = lax.conv_general_dilated(
        centered.reshape(2 * nrows, MAP, MAP, chans),
        taps,
        window_strides=(1, 1),
        padding=((half, half), (half, half)),
        dimension_numbers=("NHWC", "HWIO", "NHWC"),
        feature_group_count=chans,
        precision=lax.Precision.HIGHEST,
    ).reshape(2, nrows, npix, chans)
    total = coef + conv
    box = jnp.stack([box_center, box_radius])
    box, _ = lax.optimization_barrier((box, normed))
    box_g = lax.all_gather(box, "spec", axis=0, tiled=False)
    box_full = box_g.transpose(1, 2, 0, 3).reshape(2, npix, nsh * cl)
    center, radius = box_full[0], box_full[1]
    linear = jnp.sum(total * center, axis=(2, 3))
    spread = jnp.sum(jnp.abs(total) * radius, axis=(2, 3))
    bounds = bias + linear + jnp.stack([-spread[0], spread[1]])
    return (total[0].astype(jnp.bfloat16), total[1].astype(jnp.bfloat16), bounds.T)


def solution(mesh):
    placed = (
        P(("grp", "spec"), None, None),
        P(("grp", "spec"), None, None),
        P("spec", None),
        P("spec", None),
        P("spec"),
        P(("grp", "spec"), None, None),
        P(("grp", "spec"), None, None),
        P("grp"),
        P("grp", "spec"),
        P("grp", "spec"),
        P(None, "spec"),
        P("spec"),
        P("spec"),
        P("spec"),
        P("spec"),
        P("spec"),
    )
    return jax.shard_map(
        functools.partial(local, mesh.shape["spec"]),
        mesh=mesh,
        in_specs=placed,
        out_specs=(
            P(("grp", "spec"), None, None),
            P(("grp", "spec"), None, None),
            P(("grp", "spec"), None),
        ),
        check_vma=False,
    )
```

```python
import functools

import jax
import jax.numpy as jnp
from jax import lax
from jax.sharding import PartitionSpec as P

MAP = 14
KERNEL = 7


def conv_back(centered, taps):
    half = KERNEL // 2
    padded = jnp.pad(centered, ((0, 0), (half, half), (half, half), (0, 0)))
    result = jnp.zeros(centered.shape, jnp.float32)
    for row_off in range(KERNEL):
        for col_off in range(KERNEL):
            window = padded[
                :,
                2 * half - row_off : 2 * half - row_off + MAP,
                2 * half - col_off : 2 * half - col_off + MAP,
                :,
            ]
            result = result + window * taps[row_off, col_off]
    return result


def local(
    nsh,
    lower_coef,
    upper_coef,
    w_down,
    w_up,
    pw1_bias,
    slopes,
    intercepts,
    ln_scale,
    box_center,
    box_radius,
    dw_weight,
    dw_bias,
    ln_gain,
    ln_bias,
    ls_gamma,
    pw2_bias,
):
    nrows, npix, chans = lower_coef.shape
    hl = w_down.shape[0]
    cl = dw_bias.shape[0]
    ntap = dw_weight.shape[0]

    small = jnp.concatenate(
        [
            dw_weight,
            dw_bias[None],
            ln_gain[None],
            ln_bias[None],
            ls_gamma[None],
            pw2_bias[None],
        ],
        axis=0,
    )
    nsmall = small.shape[0]
    small_g = lax.all_gather(small, "spec", axis=0, tiled=False)
    small_full = small_g.transpose(1, 0, 2).reshape(nsmall, nsh * cl)
    kernel_taps = small_full[:ntap]
    conv_bias, gain, norm_bias, gamma, out_bias = (small_full[ntap + i] for i in range(5))

    relax = jnp.concatenate(
        [
            slopes.transpose(1, 2, 0).reshape(2 * npix, hl),
            intercepts.transpose(1, 2, 0).reshape(2 * npix, hl),
            pw1_bias[None],
        ],
        axis=0,
    )
    relax_g = lax.all_gather(relax, "spec", axis=0, tiled=False).astype(jnp.float32)

    def relax_map(i):
        return relax_g[:, i * npix : (i + 1) * npix].transpose(1, 0, 2)

    s0, s1, c0, c1 = (relax_map(i) for i in range(4))
    hid_bias = relax_g[:, 4 * npix]

    height = 2 * nrows * npix
    coef = jnp.stack([lower_coef, upper_coef]).astype(jnp.float32)
    scaled = coef * gamma
    bias = jnp.sum(scaled * out_bias, axis=(2, 3))
    flat = scaled.astype(jnp.bfloat16).reshape(height, chans)
    hidden = jnp.dot(
        flat,
        lax.all_gather(w_down, "spec", axis=0, tiled=True).T,
        preferred_element_type=jnp.float32,
    ).reshape(2, nrows, npix, nsh, hl)
    first = jnp.stack([s0, s1])[:, None]
    second = jnp.stack([s1, s0])[:, None]
    first_icpt = jnp.stack([c0, c1])[:, None]
    second_icpt = jnp.stack([c1, c0])[:, None]
    positive = jnp.maximum(hidden, 0.0)
    negative = jnp.minimum(hidden, 0.0)
    relaxed = positive * first + negative * second
    extra = jnp.sum(
        positive * first_icpt + negative * second_icpt + relaxed * hid_bias,
        axis=(2, 3, 4),
    )
    relaxed16 = relaxed.astype(jnp.bfloat16).reshape(height, -1)
    normed = jnp.dot(
        relaxed16,
        lax.all_gather(w_up, "spec", axis=0, tiled=True),
        preferred_element_type=jnp.float32,
    )
    bias = bias + extra
    normed = normed.reshape(2, nrows, npix, chans)
    bias = bias + jnp.sum(normed * norm_bias, axis=(2, 3))
    tilted = normed * gain
    centered = ln_scale[None, None, :, None] * (tilted - jnp.mean(tilted, axis=-1, keepdims=True))
    bias = bias + jnp.sum(centered * conv_bias, axis=(2, 3))
    taps = kernel_taps.reshape(KERNEL, KERNEL, 1, chans)[::-1, ::-1]
    half = KERNEL // 2
    conv = lax.conv_general_dilated(
        centered.reshape(2 * nrows, MAP, MAP, chans),
        taps,
        window_strides=(1, 1),
        padding=((half, half), (half, half)),
        dimension_numbers=("NHWC", "HWIO", "NHWC"),
        feature_group_count=chans,
        precision=lax.Precision.HIGHEST,
    ).reshape(2, nrows, npix, chans)
    total = coef + conv
    box = jnp.stack([box_center, box_radius])
    if (npix * cl) % 128 == 0:
        box = box.reshape(2, npix * cl // 128, 128)
    box, _ = lax.optimization_barrier((box, normed))
    box_g = lax.all_gather(box, "spec", axis=0, tiled=False).reshape(nsh, 2, npix, cl)
    box_full = box_g.transpose(1, 2, 0, 3).reshape(2, npix, nsh * cl)
    total, box_full = lax.optimization_barrier((total, box_full))
    center, radius = box_full[0], box_full[1]
    linear = jnp.sum(total * center, axis=(2, 3))
    spread = jnp.sum(jnp.abs(total) * radius, axis=(2, 3))
    bounds = bias + linear + jnp.stack([-spread[0], spread[1]])
    return (total[0].astype(jnp.bfloat16), total[1].astype(jnp.bfloat16), bounds.T)


def solution(mesh):
    placed = (
        P(("grp", "spec"), None, None),
        P(("grp", "spec"), None, None),
        P("spec", None),
        P("spec", None),
        P("spec"),
        P(("grp", "spec"), None, None),
        P(("grp", "spec"), None, None),
        P("grp"),
        P("grp", "spec"),
        P("grp", "spec"),
        P(None, "spec"),
        P("spec"),
        P("spec"),
        P("spec"),
        P("spec"),
        P("spec"),
    )
    return jax.shard_map(
        functools.partial(local, mesh.shape["spec"]),
        mesh=mesh,
        in_specs=placed,
        out_specs=(
            P(("grp", "spec"), None, None),
            P(("grp", "spec"), None, None),
            P(("grp", "spec"), None),
        ),
        check_vma=False,
    )
```

```python
import functools

import jax
import jax.numpy as jnp
from jax import lax
from jax.sharding import PartitionSpec as P

MAP = 14
KERNEL = 7


def conv_back(centered, taps):
    half = KERNEL // 2
    padded = jnp.pad(centered, ((0, 0), (half, half), (half, half), (0, 0)))
    result = jnp.zeros(centered.shape, jnp.float32)
    for row_off in range(KERNEL):
        for col_off in range(KERNEL):
            window = padded[
                :,
                2 * half - row_off : 2 * half - row_off + MAP,
                2 * half - col_off : 2 * half - col_off + MAP,
                :,
            ]
            result = result + window * taps[row_off, col_off]
    return result


def local(
    nsh,
    lower_coef,
    upper_coef,
    w_down,
    w_up,
    pw1_bias,
    slopes,
    intercepts,
    ln_scale,
    box_center,
    box_radius,
    dw_weight,
    dw_bias,
    ln_gain,
    ln_bias,
    ls_gamma,
    pw2_bias,
):
    nrows, npix, chans = lower_coef.shape
    hl = w_down.shape[0]
    cl = dw_bias.shape[0]
    ntap = dw_weight.shape[0]

    small = jnp.concatenate(
        [
            dw_weight,
            dw_bias[None],
            ln_gain[None],
            ln_bias[None],
            ls_gamma[None],
            pw2_bias[None],
        ],
        axis=0,
    )
    nsmall = small.shape[0]
    small_g = lax.all_gather(small, "spec", axis=0, tiled=False)
    small_full = small_g.transpose(1, 0, 2).reshape(nsmall, nsh * cl)
    kernel_taps = small_full[:ntap]
    conv_bias, gain, norm_bias, gamma, out_bias = (small_full[ntap + i] for i in range(5))

    gi = lax.axis_index("grp")
    half = hl // 2

    def halves(a):
        own = lax.dynamic_slice_in_dim(a, gi * half, half, 0)
        other = lax.dynamic_slice_in_dim(a, (1 - gi) * half, half, 0)
        return own, other

    swap = [(0, 1), (1, 0)]
    down_own = lax.all_gather(halves(w_down)[0], "spec", axis=0, tiled=True)
    up_own = lax.all_gather(halves(w_up)[0], "spec", axis=0, tiled=True)
    down_other = lax.ppermute(down_own, "grp", swap)
    up_other = lax.ppermute(up_own, "grp", swap)

    def relax_pack(sl, ic, hb):
        return jnp.concatenate(
            [
                sl.transpose(1, 2, 0).reshape(2 * npix, half),
                ic.transpose(1, 2, 0).reshape(2 * npix, half),
                hb[None],
            ],
            axis=0,
        )

    sl_h, ic_h, hb_h = halves(slopes), halves(intercepts), halves(pw1_bias)
    relax = jnp.stack([relax_pack(sl_h[i], ic_h[i], hb_h[i]) for i in range(2)])
    relax_g = lax.all_gather(relax, "spec", axis=0, tiled=False).astype(jnp.float32)

    height = 2 * nrows * npix
    coef = jnp.stack([lower_coef, upper_coef]).astype(jnp.float32)
    scaled = coef * gamma
    bias = jnp.sum(scaled * out_bias, axis=(2, 3))
    flat = scaled.astype(jnp.bfloat16).reshape(height, chans)

    def relax_half(h, w_dn, w_u):
        rg = relax_g[:, h]

        def relax_map(i):
            return rg[:, i * npix : (i + 1) * npix].transpose(1, 0, 2)

        s0, s1, c0, c1 = (relax_map(i) for i in range(4))
        hid_bias = rg[:, 4 * npix]
        hidden = jnp.dot(flat, w_dn.T, preferred_element_type=jnp.float32).reshape(
            2, nrows, npix, nsh, half
        )
        first = jnp.stack([s0, s1])[:, None]
        second = jnp.stack([s1, s0])[:, None]
        first_icpt = jnp.stack([c0, c1])[:, None]
        second_icpt = jnp.stack([c1, c0])[:, None]
        positive = jnp.maximum(hidden, 0.0)
        negative = jnp.minimum(hidden, 0.0)
        relaxed = positive * first + negative * second
        part = jnp.sum(
            positive * first_icpt + negative * second_icpt + relaxed * hid_bias,
            axis=(2, 3, 4),
        )
        relaxed16 = relaxed.astype(jnp.bfloat16).reshape(height, -1)
        return jnp.dot(relaxed16, w_u, preferred_element_type=jnp.float32), part

    normed_a, extra_a = relax_half(0, down_own, up_own)
    normed_b, extra_b = relax_half(1, down_other, up_other)
    normed = normed_a + normed_b
    extra = extra_a + extra_b
    bias = bias + extra
    normed = normed.reshape(2, nrows, npix, chans)
    box = jnp.stack([box_center, box_radius])
    if (npix * cl) % 128 == 0:
        box = box.reshape(2, npix * cl // 128, 128)
    box, normed = lax.optimization_barrier((box, normed))
    bias = bias + jnp.sum(normed * norm_bias, axis=(2, 3))
    tilted = normed * gain
    centered = ln_scale[None, None, :, None] * (tilted - jnp.mean(tilted, axis=-1, keepdims=True))
    bias = bias + jnp.sum(centered * conv_bias, axis=(2, 3))
    taps = kernel_taps.reshape(KERNEL, KERNEL, 1, chans)[::-1, ::-1]
    half = KERNEL // 2
    conv = lax.conv_general_dilated(
        centered.reshape(2 * nrows, MAP, MAP, chans),
        taps,
        window_strides=(1, 1),
        padding=((half, half), (half, half)),
        dimension_numbers=("NHWC", "HWIO", "NHWC"),
        feature_group_count=chans,
        precision=lax.Precision.HIGHEST,
    ).reshape(2, nrows, npix, chans)
    total = coef + conv
    box_g = lax.all_gather(box, "spec", axis=0, tiled=False).reshape(nsh, 2, npix, cl)
    box_full = box_g.transpose(1, 2, 0, 3).reshape(2, npix, nsh * cl)
    total, box_full = lax.optimization_barrier((total, box_full))
    center, radius = box_full[0], box_full[1]
    linear = jnp.sum(total * center, axis=(2, 3))
    spread = jnp.sum(jnp.abs(total) * radius, axis=(2, 3))
    bounds = bias + linear + jnp.stack([-spread[0], spread[1]])
    return (total[0].astype(jnp.bfloat16), total[1].astype(jnp.bfloat16), bounds.T)


def solution(mesh):
    placed = (
        P(("grp", "spec"), None, None),
        P(("grp", "spec"), None, None),
        P("spec", None),
        P("spec", None),
        P("spec"),
        P(("grp", "spec"), None, None),
        P(("grp", "spec"), None, None),
        P("grp"),
        P("grp", "spec"),
        P("grp", "spec"),
        P(None, "spec"),
        P("spec"),
        P("spec"),
        P("spec"),
        P("spec"),
        P("spec"),
    )
    return jax.shard_map(
        functools.partial(local, mesh.shape["spec"]),
        mesh=mesh,
        in_specs=placed,
        out_specs=(
            P(("grp", "spec"), None, None),
            P(("grp", "spec"), None, None),
            P(("grp", "spec"), None),
        ),
        check_vma=False,
    )
```

```python
import functools

import jax
import jax.numpy as jnp
from jax import lax
from jax.sharding import PartitionSpec as P

MAP = 14
KERNEL = 7


def conv_back(centered, taps):
    half = KERNEL // 2
    padded = jnp.pad(centered, ((0, 0), (half, half), (half, half), (0, 0)))
    result = jnp.zeros(centered.shape, jnp.float32)
    for row_off in range(KERNEL):
        for col_off in range(KERNEL):
            window = padded[
                :,
                2 * half - row_off : 2 * half - row_off + MAP,
                2 * half - col_off : 2 * half - col_off + MAP,
                :,
            ]
            result = result + window * taps[row_off, col_off]
    return result


def local(
    nsh,
    lower_coef,
    upper_coef,
    w_down,
    w_up,
    pw1_bias,
    slopes,
    intercepts,
    ln_scale,
    box_center,
    box_radius,
    dw_weight,
    dw_bias,
    ln_gain,
    ln_bias,
    ls_gamma,
    pw2_bias,
):
    nrows, npix, chans = lower_coef.shape
    hl = w_down.shape[0]
    cl = dw_bias.shape[0]
    ntap = dw_weight.shape[0]

    small = jnp.concatenate(
        [
            dw_weight,
            dw_bias[None],
            ln_gain[None],
            ln_bias[None],
            ls_gamma[None],
            pw2_bias[None],
        ],
        axis=0,
    )
    nsmall = small.shape[0]
    small_g = lax.all_gather(small, "spec", axis=0, tiled=False)
    small_full = small_g.transpose(1, 0, 2).reshape(nsmall, nsh * cl)
    kernel_taps = small_full[:ntap]
    conv_bias, gain, norm_bias, gamma, out_bias = (small_full[ntap + i] for i in range(5))

    relax = jnp.concatenate(
        [
            slopes.transpose(1, 2, 0).reshape(2 * npix, hl),
            intercepts.transpose(1, 2, 0).reshape(2 * npix, hl),
            pw1_bias[None],
        ],
        axis=0,
    )
    nrelax = relax.shape[0]

    def rows_of(flat):
        pad = (-flat.shape[0]) % chans
        return jnp.pad(flat, (0, pad)).reshape(-1, chans)

    pack1 = jnp.concatenate([w_down, rows_of(relax.reshape(-1))], axis=0)
    gath1 = lax.all_gather(pack1, "spec", axis=0, tiled=False)
    wd_full = gath1[:, :hl].reshape(nsh * hl, chans)
    relax_g = (
        gath1[:, hl:]
        .reshape(nsh, -1)[:, : nrelax * hl]
        .reshape(nsh, nrelax, hl)
        .astype(jnp.float32)
    )

    box = jnp.stack([box_center, box_radius])
    box_hi = lax.reduce_precision(box, exponent_bits=8, mantissa_bits=7)
    box_rest = box - box_hi
    box_mid = lax.reduce_precision(box_rest, exponent_bits=8, mantissa_bits=7)
    box_lo = box_rest - box_mid
    box_parts = jnp.stack([box_hi, box_mid, box_lo]).astype(jnp.bfloat16)
    nbox = box_parts.size
    pack2 = jnp.concatenate([w_up, rows_of(box_parts.reshape(-1))], axis=0)
    pack2, gath1 = lax.optimization_barrier((pack2, gath1))
    gath2 = lax.all_gather(pack2, "spec", axis=0, tiled=False)
    wu_full = gath2[:, :hl].reshape(nsh * hl, chans)
    box_g = (
        gath2[:, hl:]
        .reshape(nsh, -1)[:, :nbox]
        .reshape(nsh, 3, 2, npix, cl)
        .astype(jnp.float32)
    )
    box_g = (box_g[:, 0] + box_g[:, 1]) + box_g[:, 2]

    def relax_map(i):
        return relax_g[:, i * npix : (i + 1) * npix].transpose(1, 0, 2)

    s0, s1, c0, c1 = (relax_map(i) for i in range(4))
    hid_bias = relax_g[:, 4 * npix]

    height = 2 * nrows * npix
    coef = jnp.stack([lower_coef, upper_coef]).astype(jnp.float32)
    scaled = coef * gamma
    bias = jnp.sum(scaled * out_bias, axis=(2, 3))
    flat = scaled.astype(jnp.bfloat16).reshape(height, chans)
    hidden = jnp.dot(
        flat,
        wd_full.T,
        preferred_element_type=jnp.float32,
    ).reshape(2, nrows, npix, nsh, hl)
    first = jnp.stack([s0, s1])[:, None]
    second = jnp.stack([s1, s0])[:, None]
    first_icpt = jnp.stack([c0, c1])[:, None]
    second_icpt = jnp.stack([c1, c0])[:, None]
    positive = jnp.maximum(hidden, 0.0)
    negative = jnp.minimum(hidden, 0.0)
    relaxed = positive * first + negative * second
    extra = jnp.sum(
        positive * first_icpt + negative * second_icpt + relaxed * hid_bias,
        axis=(2, 3, 4),
    )
    relaxed16 = relaxed.astype(jnp.bfloat16).reshape(height, -1)
    normed = jnp.dot(
        relaxed16,
        wu_full,
        preferred_element_type=jnp.float32,
    )
    bias = bias + extra
    normed = normed.reshape(2, nrows, npix, chans)
    bias = bias + jnp.sum(normed * norm_bias, axis=(2, 3))
    tilted = normed * gain
    centered = ln_scale[None, None, :, None] * (tilted - jnp.mean(tilted, axis=-1, keepdims=True))
    bias = bias + jnp.sum(centered * conv_bias, axis=(2, 3))
    taps = kernel_taps.reshape(KERNEL, KERNEL, 1, chans)[::-1, ::-1]
    half = KERNEL // 2
    conv = lax.conv_general_dilated(
        centered.reshape(2 * nrows, MAP, MAP, chans),
        taps,
        window_strides=(1, 1),
        padding=((half, half), (half, half)),
        dimension_numbers=("NHWC", "HWIO", "NHWC"),
        feature_group_count=chans,
        precision=lax.Precision.HIGHEST,
    ).reshape(2, nrows, npix, chans)
    total = coef + conv
    box_full = box_g.transpose(1, 2, 0, 3).reshape(2, npix, nsh * cl)
    total, box_full = lax.optimization_barrier((total, box_full))
    center, radius = box_full[0], box_full[1]
    linear = jnp.sum(total * center, axis=(2, 3))
    spread = jnp.sum(jnp.abs(total) * radius, axis=(2, 3))
    bounds = bias + linear + jnp.stack([-spread[0], spread[1]])
    return (total[0].astype(jnp.bfloat16), total[1].astype(jnp.bfloat16), bounds.T)


def solution(mesh):
    placed = (
        P(("grp", "spec"), None, None),
        P(("grp", "spec"), None, None),
        P("spec", None),
        P("spec", None),
        P("spec"),
        P(("grp", "spec"), None, None),
        P(("grp", "spec"), None, None),
        P("grp"),
        P("grp", "spec"),
        P("grp", "spec"),
        P(None, "spec"),
        P("spec"),
        P("spec"),
        P("spec"),
        P("spec"),
        P("spec"),
    )
    return jax.shard_map(
        functools.partial(local, mesh.shape["spec"]),
        mesh=mesh,
        in_specs=placed,
        out_specs=(
            P(("grp", "spec"), None, None),
            P(("grp", "spec"), None, None),
            P(("grp", "spec"), None),
        ),
        check_vma=False,
    )
```

```python
import functools

import jax
import jax.numpy as jnp
from jax import lax
from jax.sharding import PartitionSpec as P

MAP = 14
KERNEL = 7


def conv_back(centered, taps):
    half = KERNEL // 2
    padded = jnp.pad(centered, ((0, 0), (half, half), (half, half), (0, 0)))
    result = jnp.zeros(centered.shape, jnp.float32)
    for row_off in range(KERNEL):
        for col_off in range(KERNEL):
            window = padded[
                :,
                2 * half - row_off : 2 * half - row_off + MAP,
                2 * half - col_off : 2 * half - col_off + MAP,
                :,
            ]
            result = result + window * taps[row_off, col_off]
    return result


def local(
    nsh,
    lower_coef,
    upper_coef,
    w_down,
    w_up,
    pw1_bias,
    slopes,
    intercepts,
    ln_scale,
    box_center,
    box_radius,
    dw_weight,
    dw_bias,
    ln_gain,
    ln_bias,
    ls_gamma,
    pw2_bias,
):
    nrows, npix, chans = lower_coef.shape
    hl = w_down.shape[0]
    cl = dw_bias.shape[0]
    ntap = dw_weight.shape[0]

    small = jnp.concatenate(
        [
            dw_weight,
            dw_bias[None],
            ln_gain[None],
            ln_bias[None],
            ls_gamma[None],
            pw2_bias[None],
        ],
        axis=0,
    )
    nsmall = small.shape[0]
    small_g = lax.all_gather(small, "spec", axis=0, tiled=False)
    small_full = small_g.transpose(1, 0, 2).reshape(nsmall, nsh * cl)
    kernel_taps = small_full[:ntap]
    conv_bias, gain, norm_bias, gamma, out_bias = (small_full[ntap + i] for i in range(5))

    relax = jnp.concatenate(
        [
            slopes.reshape(hl, 2 * npix),
            intercepts.reshape(hl, 2 * npix),
            pw1_bias[:, None],
        ],
        axis=1,
    )
    nrel = relax.shape[1]

    box = jnp.stack([box_center, box_radius])
    box_hi = lax.reduce_precision(box, exponent_bits=8, mantissa_bits=7)
    box_rest = box - box_hi
    box_mid = lax.reduce_precision(box_rest, exponent_bits=8, mantissa_bits=7)
    box_lo = box_rest - box_mid
    box_flat = jnp.stack([box_hi, box_mid, box_lo]).astype(jnp.bfloat16).reshape(-1)
    nbox = box_flat.shape[0]
    box_cols = jnp.pad(box_flat, (0, (-nbox) % hl)).reshape(hl, -1)
    nbc = box_cols.shape[1]

    pack1 = jnp.concatenate([w_down, relax, box_cols], axis=1)
    gath1 = lax.all_gather(pack1, "spec", axis=0, tiled=True)
    wd_full = gath1[:, :chans]
    rel_g = gath1[:, chans : chans + nrel].astype(jnp.float32)
    box_g = (
        gath1[:, chans + nrel :]
        .reshape(nsh, hl * nbc)[:, :nbox]
        .reshape(nsh, 3, 2, npix, cl)
        .astype(jnp.float32)
    )
    box_g = (box_g[:, 0] + box_g[:, 1]) + box_g[:, 2]
    up_in, gath1 = lax.optimization_barrier((w_up, gath1))
    wu_full = lax.all_gather(up_in, "spec", axis=0, tiled=True)

    sl = rel_g[:, : 2 * npix].reshape(-1, 2, npix)
    ic = rel_g[:, 2 * npix : 4 * npix].reshape(-1, 2, npix)
    hid_bias = rel_g[:, 4 * npix][:, None]

    coef = jnp.stack([lower_coef, upper_coef]).astype(jnp.float32)
    scaled = coef * gamma
    bias = jnp.sum(scaled * out_bias, axis=(2, 3))
    scaled16 = scaled.astype(jnp.bfloat16)

    normed_rows = []
    extra_rows = []
    for s in range(2):
        first, second = sl[:, s], sl[:, 1 - s]
        first_icpt, second_icpt = ic[:, s], ic[:, 1 - s]
        for r in range(nrows):
            hidden_t = lax.dot_general(
                wd_full,
                scaled16[s, r],
                (((1,), (1,)), ((), ())),
                preferred_element_type=jnp.float32,
            )
            positive = jnp.maximum(hidden_t, 0.0)
            negative = jnp.minimum(hidden_t, 0.0)
            relaxed_t = positive * first + negative * second
            extra_rows.append(
                jnp.sum(
                    positive * first_icpt
                    + negative * second_icpt
                    + relaxed_t * hid_bias
                )
            )
            normed_rows.append(
                lax.dot_general(
                    relaxed_t.astype(jnp.bfloat16),
                    wu_full,
                    (((0,), (0,)), ((), ())),
                    preferred_element_type=jnp.float32,
                )
            )
    normed = jnp.stack(normed_rows).reshape(2, nrows, npix, chans)
    extra = jnp.stack(extra_rows).reshape(2, nrows)
    bias = bias + extra
    bias = bias + jnp.sum(normed * norm_bias, axis=(2, 3))
    tilted = normed * gain
    centered = ln_scale[None, None, :, None] * (tilted - jnp.mean(tilted, axis=-1, keepdims=True))
    bias = bias + jnp.sum(centered * conv_bias, axis=(2, 3))
    taps = kernel_taps.reshape(KERNEL, KERNEL, 1, chans)[::-1, ::-1]
    half = KERNEL // 2
    conv = lax.conv_general_dilated(
        centered.reshape(2 * nrows, MAP, MAP, chans),
        taps,
        window_strides=(1, 1),
        padding=((half, half), (half, half)),
        dimension_numbers=("NHWC", "HWIO", "NHWC"),
        feature_group_count=chans,
        precision=lax.Precision.HIGHEST,
    ).reshape(2, nrows, npix, chans)
    total = coef + conv
    box_full = box_g.transpose(1, 2, 0, 3).reshape(2, npix, nsh * cl)
    total, box_full = lax.optimization_barrier((total, box_full))
    center, radius = box_full[0], box_full[1]
    linear = jnp.sum(total * center, axis=(2, 3))
    spread = jnp.sum(jnp.abs(total) * radius, axis=(2, 3))
    bounds = bias + linear + jnp.stack([-spread[0], spread[1]])
    return (total[0].astype(jnp.bfloat16), total[1].astype(jnp.bfloat16), bounds.T)


def solution(mesh):
    placed = (
        P(("grp", "spec"), None, None),
        P(("grp", "spec"), None, None),
        P("spec", None),
        P("spec", None),
        P("spec"),
        P(("grp", "spec"), None, None),
        P(("grp", "spec"), None, None),
        P("grp"),
        P("grp", "spec"),
        P("grp", "spec"),
        P(None, "spec"),
        P("spec"),
        P("spec"),
        P("spec"),
        P("spec"),
        P("spec"),
    )
    return jax.shard_map(
        functools.partial(local, mesh.shape["spec"]),
        mesh=mesh,
        in_specs=placed,
        out_specs=(
            P(("grp", "spec"), None, None),
            P(("grp", "spec"), None, None),
            P(("grp", "spec"), None),
        ),
        check_vma=False,
    )
```

```python
import functools

import jax
import jax.numpy as jnp
from jax import lax
from jax.sharding import PartitionSpec as P

MAP = 14
KERNEL = 7


def conv_back(centered, taps):
    half = KERNEL // 2
    padded = jnp.pad(centered, ((0, 0), (half, half), (half, half), (0, 0)))
    result = jnp.zeros(centered.shape, jnp.float32)
    for row_off in range(KERNEL):
        for col_off in range(KERNEL):
            window = padded[
                :,
                2 * half - row_off : 2 * half - row_off + MAP,
                2 * half - col_off : 2 * half - col_off + MAP,
                :,
            ]
            result = result + window * taps[row_off, col_off]
    return result


def local(
    nsh,
    lower_coef,
    upper_coef,
    w_down,
    w_up,
    pw1_bias,
    slopes,
    intercepts,
    ln_scale,
    box_center,
    box_radius,
    dw_weight,
    dw_bias,
    ln_gain,
    ln_bias,
    ls_gamma,
    pw2_bias,
):
    nrows, npix, chans = lower_coef.shape
    hl = w_down.shape[0]
    cl = dw_bias.shape[0]
    ntap = dw_weight.shape[0]

    relax = jnp.concatenate(
        [
            slopes.reshape(hl, 2 * npix),
            intercepts.reshape(hl, 2 * npix),
            pw1_bias[:, None],
        ],
        axis=1,
    )
    nrel = relax.shape[1]

    small = jnp.concatenate(
        [
            box_center,
            box_radius,
            dw_weight,
            dw_bias[None],
            ln_gain[None],
            ln_bias[None],
            ls_gamma[None],
            pw2_bias[None],
        ],
        axis=0,
    )
    nsmall = small.shape[0]
    small_hi = lax.reduce_precision(small, exponent_bits=8, mantissa_bits=7)
    small_rest = small - small_hi
    small_mid = lax.reduce_precision(small_rest, exponent_bits=8, mantissa_bits=7)
    small_lo = small_rest - small_mid
    small_flat = jnp.stack([small_hi, small_mid, small_lo]).astype(jnp.bfloat16).reshape(-1)
    nbox = small_flat.shape[0]
    box_cols = jnp.pad(small_flat, (0, (-nbox) % hl)).reshape(hl, -1)
    nbc = box_cols.shape[1]

    pack1 = jnp.concatenate([w_down, w_up, relax, box_cols], axis=1)
    gath1 = lax.all_gather(pack1, "spec", axis=0, tiled=True)
    wd_full = gath1[:, :chans]
    wu_full = gath1[:, chans : 2 * chans]
    gath1 = gath1[:, chans:]
    small_g = (
        gath1[:, chans + nrel :]
        .reshape(nsh, hl * nbc)[:, :nbox]
        .reshape(nsh, 3, nsmall, cl)
        .astype(jnp.float32)
    )
    small_g = (small_g[:, 0] + small_g[:, 1]) + small_g[:, 2]
    small_full = small_g.transpose(1, 0, 2).reshape(nsmall, nsh * cl)
    o = 0
    center = small_full[o : o + npix]
    o += npix
    radius = small_full[o : o + npix]
    o += npix
    kernel_taps = small_full[o : o + ntap]
    o += ntap
    conv_bias, gain, norm_bias, gamma, out_bias = (small_full[o + i] for i in range(5))

    coef = jnp.stack([lower_coef, upper_coef]).astype(jnp.float32)
    scaled = coef * gamma
    bias = jnp.sum(scaled * out_bias, axis=(2, 3))
    flat = scaled.astype(jnp.bfloat16).reshape(2 * nrows * npix, chans)
    hidden_t = lax.dot_general(
        wd_full, flat, (((1,), (1,)), ((), ())), preferred_element_type=jnp.float32
    )

    def rel_cols(i):
        return gath1[:, chans + i * npix : chans + (i + 1) * npix].astype(jnp.float32)

    hid_bias = gath1[:, chans + 4 * npix : chans + 4 * npix + 1].astype(jnp.float32)
    pieces = []
    extra_rows = []
    for s in range(2):
        first, second = rel_cols(s), rel_cols(1 - s)
        first_icpt, second_icpt = rel_cols(2 + s), rel_cols(3 - s)
        for r in range(nrows):
            k = s * nrows + r
            h = hidden_t[:, k * npix : (k + 1) * npix]
            positive = jnp.maximum(h, 0.0)
            negative = jnp.minimum(h, 0.0)
            relaxed_t = positive * first + negative * second
            extra_rows.append(
                jnp.sum(
                    positive * first_icpt
                    + negative * second_icpt
                    + relaxed_t * hid_bias
                )
            )
            pieces.append(relaxed_t.astype(jnp.bfloat16))
    relaxed16_t = jnp.concatenate(pieces, axis=1)
    normed = lax.dot_general(
        relaxed16_t, wu_full, (((0,), (0,)), ((), ())), preferred_element_type=jnp.float32
    ).reshape(2, nrows, npix, chans)
    extra = jnp.stack(extra_rows).reshape(2, nrows)
    bias = bias + extra
    bias = bias + jnp.sum(normed * norm_bias, axis=(2, 3))
    tilted = normed * gain
    centered = ln_scale[None, None, :, None] * (tilted - jnp.mean(tilted, axis=-1, keepdims=True))
    bias = bias + jnp.sum(centered * conv_bias, axis=(2, 3))
    taps = kernel_taps.reshape(KERNEL, KERNEL, 1, chans)[::-1, ::-1]
    half = KERNEL // 2
    conv = lax.conv_general_dilated(
        centered.reshape(2 * nrows, MAP, MAP, chans),
        taps,
        window_strides=(1, 1),
        padding=((half, half), (half, half)),
        dimension_numbers=("NHWC", "HWIO", "NHWC"),
        feature_group_count=chans,
        precision=lax.Precision.HIGHEST,
    ).reshape(2, nrows, npix, chans)
    total = coef + conv
    linear = jnp.sum(total * center, axis=(2, 3))
    spread = jnp.sum(jnp.abs(total) * radius, axis=(2, 3))
    bounds = bias + linear + jnp.stack([-spread[0], spread[1]])
    return (total[0].astype(jnp.bfloat16), total[1].astype(jnp.bfloat16), bounds.T)


def solution(mesh):
    placed = (
        P(("grp", "spec"), None, None),
        P(("grp", "spec"), None, None),
        P("spec", None),
        P("spec", None),
        P("spec"),
        P(("grp", "spec"), None, None),
        P(("grp", "spec"), None, None),
        P("grp"),
        P("grp", "spec"),
        P("grp", "spec"),
        P(None, "spec"),
        P("spec"),
        P("spec"),
        P("spec"),
        P("spec"),
        P("spec"),
    )
    return jax.shard_map(
        functools.partial(local, mesh.shape["spec"]),
        mesh=mesh,
        in_specs=placed,
        out_specs=(
            P(("grp", "spec"), None, None),
            P(("grp", "spec"), None, None),
            P(("grp", "spec"), None),
        ),
        check_vma=False,
    )
```
